512 devices in a mesh: dp: 64 (over x_hi, z, core), tp: 8 (over x_lo, y).
Axes of the slice: x: 4 (x_hi: 2, x_lo: 2; x = x_hi * 2 + x_lo), y: 4, z: 16, core: 2. Of those that a mesh axis runs over, the one named last changes fastest.
Arguments:
- decode_step_input: bfloat16 [2, 64, 8192], P(None, 'dp'), may hold values from -6 to 6
- query_key_value_weight: bfloat16 [8192, 10240], P('dp', 'tp'), may hold values from -0.0625 to 0.0625
- stored_keys: bfloat16 [64, 256, 1024], P('dp', None, 'tp'), may hold values from -240 to 240
- stored_values: bfloat16 [64, 256, 1024], P('dp', None, 'tp'), may hold values from -6 to 6
- stored_lengths: int32 [64], P('dp'), may hold values from 1 to 256
- pooled_layer_input: bfloat16 [768, 16, 8192], P('dp', None, 'tp'), may hold values from -6 to 6
- pooled_value_gradient: bfloat16 [768, 16, 1024], P('dp', None, 'tp'), may hold values from -6 to 6
- finished: int32 [768], P('dp'), may hold values from 0 to 1
- sequence_token_count: int32 [768], P('dp'), may hold values from 1 to 16
- destinations: int32 [768], P('dp'), may hold values from 0 to 63, as said below
- advantages: float32 [768], P('dp'), may hold values from -4 to 4
- frozen_value_weight: bfloat16 [8192, 1024], P(None, 'tp'), may hold values from -0.0625 to 0.0625
- adapter_down_weight: bfloat16 [8192, 64], replicated, may hold values from -0.0625 to 0.0625
- adapter_up_weight: bfloat16 [64, 1024], P(None, 'tp'), may hold values from -0.75 to 0.75
Outputs:
- decode_mix: bfloat16 [2, 64, 8192], P(None, 'dp', 'tp')
- trainer_value_rows: bfloat16 [12288, 1024], P('dp', 'tp')
- grad_down: float32 [8, 1024, 64], P('tp', 'dp')
- grad_up: float32 [64, 1024], P(None, 'tp')
The draws below stay inside these ranges and needn't reach their ends.
Inputs may be any that keep to these rules, and one draw needn't show every extreme that they name: `destinations`: every replica sends exactly 3 of its pooled sequences to each of the learner shards r, r + 1, ..., r + 4 - 1 (mod the dp axis's size), where r is the replica's index.
All inputs are finite; a program needn't handle non-finite values.
Results may differ from the reference program's by a relative error of at most 0.017.
Values may be sent and summed in bfloat16 or wider, within the bound.
No kernel may reach another device: no remote copies, remote signals or barrier semaphores. Data moves between devices by JAX's collectives and lax.ppermute only.
A program may use at most 64 MiB of HBM per device.

```python
import jax
import jax.numpy as jnp
from jax import lax

MODEL_WIDTH = 8192
HQ = 64
KEY_VALUE_HEADS = 8
HEAD_SIZE = 128
ADAPTER_RANK = 64
DECODE_STEPS = 2
OFFS = 4
SLOTS = 3
CACHE_POSITIONS = 256
POOLED_LENGTH = 16
QUERY_GROUP = 8
DECODE_SEQUENCES = 64
POOL = 12
POOLED_SEQUENCES = 768
LEARNER_TOKENS = 12288
N_DP = 64
N_TP = 8


def relay_tables(key):
    seeded = jax.random.fold_in(key, 11)
    order_key, count_key, pick_key, finish_key = jax.random.split(seeded, 4)
    replicas = POOLED_SEQUENCES // POOL
    pattern = jnp.repeat(jnp.arange(OFFS, dtype=jnp.int32), SLOTS)
    shuffled = jax.random.permutation(order_key, jnp.tile(pattern[None, :], (replicas, 1)), axis=1, independent=True)
    owners = jnp.arange(replicas, dtype=jnp.int32)[:, None]
    targets = ((owners + shuffled) % replicas).reshape(POOLED_SEQUENCES).astype(jnp.int32)
    counts = jax.random.randint(count_key, (replicas, POOL), max(POOLED_LENGTH // 4, 1), POOLED_LENGTH + 1)
    chosen = jax.random.randint(pick_key, (replicas, 1), 0, POOL)
    column = jnp.arange(POOL, dtype=jnp.int32)[None, :]
    counts = jnp.where(column == chosen, POOLED_LENGTH, counts).reshape(POOLED_SEQUENCES).astype(jnp.int32)
    flags = jax.random.randint(finish_key, (replicas, POOL), 0, 4) > 0
    flags = jnp.where(column == chosen, True, flags).reshape(POOLED_SEQUENCES).astype(jnp.int32)
    return (targets, counts, flags)


def draw_destinations(key, part):
    return relay_tables(key)[0]


def draw_sequence_token_count(key, part):
    return relay_tables(key)[1]


def draw_finished(key, part):
    return relay_tables(key)[2]


def draw_stored_lengths(key, part):
    length_key, pick_key = jax.random.split(jax.random.fold_in(key, 23))
    lengths = jax.random.randint(length_key, (DECODE_SEQUENCES,), 1, CACHE_POSITIONS + 1)
    chosen = jax.random.randint(pick_key, (), 0, DECODE_SEQUENCES)
    return jnp.where(jnp.arange(DECODE_SEQUENCES) == chosen, CACHE_POSITIONS, lengths).astype(jnp.int32)


def draw_stored_keys(key, part):
    value_random_key = jax.random.fold_in(jax.random.fold_in(key, 31), 0)
    table_entries = jnp.clip(jax.random.normal(value_random_key, (DECODE_SEQUENCES, CACHE_POSITIONS, KEY_VALUE_HEADS * HEAD_SIZE), jnp.float32), -6.0, 6.0)
    return table_entries.astype(jnp.bfloat16)


def steps_of(key, dims, cuts, smallest, high):
    def one(dim, parts):
        steps = jax.random.uniform(jax.random.fold_in(jax.random.fold_in(key, 6), dim), (parts,), jnp.float32, smallest / len(cuts), high / len(cuts))
        return jnp.repeat(jnp.exp(steps), dims[dim] // parts).reshape((-1,) + (1,) * (len(dims) - dim - 1))

    factor_of = one(*cuts[0])
    for cut in cuts[1:]:
        factor_of = factor_of * one(*cut)
    return factor_of


def bell_draw(own_key, dims, width, reach, shards=(), kind=jnp.bfloat16):
    drawn = jax.random.normal(own_key, dims, jnp.float32) * width
    if len(shards) > 0:
        drawn = steps_of(own_key, dims, shards, -0.22, 0.18) * drawn
    return jnp.clip(drawn, min=-reach, max=reach).astype(kind)


def setup_inputs(seed: int = 0) -> dict:
    streams_of = jax.random.split(jax.random.key(seed), 15)
    return {
        "decode_step_input": bell_draw(streams_of[0], (DECODE_STEPS, DECODE_SEQUENCES, MODEL_WIDTH), 1.0, 6.0, ((1, 64),)),
        "query_key_value_weight": bell_draw(streams_of[1], (MODEL_WIDTH, KEY_VALUE_HEADS * (QUERY_GROUP + 2) * HEAD_SIZE), MODEL_WIDTH ** -0.5, 0.0625, ((0, 64), (1, 8))),
        "stored_keys": draw_stored_keys(jax.random.fold_in(streams_of[14], 71), 0),
        "stored_values": bell_draw(streams_of[3], (DECODE_SEQUENCES, CACHE_POSITIONS, KEY_VALUE_HEADS * HEAD_SIZE), 1.0, 6.0, ((0, 64), (2, 8))),
        "stored_lengths": draw_stored_lengths(jax.random.fold_in(streams_of[14], 71), 0),
        "pooled_layer_input": bell_draw(streams_of[5], (POOLED_SEQUENCES, POOLED_LENGTH, MODEL_WIDTH), 1.0, 6.0, ((0, 64), (2, 8))),
        "pooled_value_gradient": bell_draw(streams_of[6], (POOLED_SEQUENCES, POOLED_LENGTH, KEY_VALUE_HEADS * HEAD_SIZE), 1.0, 6.0, ((0, 64), (2, 8))),
        "finished": draw_finished(jax.random.fold_in(streams_of[14], 71), 0),
        "sequence_token_count": draw_sequence_token_count(jax.random.fold_in(streams_of[14], 71), 0),
        "destinations": draw_destinations(jax.random.fold_in(streams_of[14], 71), 0),
        "advantages": bell_draw(streams_of[10], (POOLED_SEQUENCES,), 1.0, 4.0, ((0, 64),), jnp.float32),
        "frozen_value_weight": bell_draw(streams_of[11], (MODEL_WIDTH, KEY_VALUE_HEADS * HEAD_SIZE), MODEL_WIDTH ** -0.5, 0.0625, ((1, 8),)),
        "adapter_down_weight": bell_draw(streams_of[12], (MODEL_WIDTH, ADAPTER_RANK), MODEL_WIDTH ** -0.5, 0.0625),
        "adapter_up_weight": bell_draw(streams_of[13], (ADAPTER_RANK, KEY_VALUE_HEADS * HEAD_SIZE), ADAPTER_RANK ** -0.5, 0.75, ((1, 8),)),
    }


def reference(decode_step_input, query_key_value_weight, stored_keys, stored_values, stored_lengths, pooled_layer_input, pooled_value_gradient, finished, sequence_token_count, destinations, advantages, frozen_value_weight, adapter_down_weight, adapter_up_weight):
    flat_inputs = decode_step_input.reshape(DECODE_STEPS * DECODE_SEQUENCES, MODEL_WIDTH)
    projected_rows = jnp.dot(flat_inputs, query_key_value_weight, preferred_element_type=jnp.float32).astype(jnp.bfloat16)
    projected_rows = projected_rows.reshape(DECODE_STEPS, DECODE_SEQUENCES, KEY_VALUE_HEADS, QUERY_GROUP + 2, HEAD_SIZE).astype(jnp.float32)
    queries = projected_rows[:, :, :, :QUERY_GROUP, :]
    new_keys = projected_rows[:, :, :, QUERY_GROUP, :]
    new_values = projected_rows[:, :, :, QUERY_GROUP + 1, :]
    previous_keys = stored_keys.reshape(DECODE_SEQUENCES, CACHE_POSITIONS, KEY_VALUE_HEADS, HEAD_SIZE).astype(jnp.float32)
    previous_values = stored_values.reshape(DECODE_SEQUENCES, CACHE_POSITIONS, KEY_VALUE_HEADS, HEAD_SIZE).astype(jnp.float32)
    scale = 1.0 / jnp.sqrt(jnp.float32(HEAD_SIZE))
    cached = jnp.einsum('tbhgd,bphd->tbhgp', queries, previous_keys) * scale
    valid = jnp.arange(CACHE_POSITIONS, dtype=jnp.int32)[None, :] < stored_lengths[:, None]
    cached = jnp.where(valid[None, :, None, None, :], cached, jnp.float32(-1e+30))
    recent = jnp.einsum('tbhgd,ubhd->tbhgu', queries, new_keys) * scale
    causal = jnp.arange(DECODE_STEPS, dtype=jnp.int32)[None, :] <= jnp.arange(DECODE_STEPS, dtype=jnp.int32)[:, None]
    recent = jnp.where(causal[:, None, None, None, :], recent, jnp.float32(-1e+30))
    scores = jnp.concatenate([cached, recent], axis=-1)
    highest = lax.optimization_barrier(jnp.max(scores, axis=-1, keepdims=True))
    expo = jnp.exp(scores - highest)
    weights = (expo / lax.optimization_barrier(jnp.sum(expo, axis=-1, keepdims=True))).astype(jnp.bfloat16).astype(jnp.float32)
    mixed = jnp.einsum('tbhgp,bphd->tbhgd', weights[..., :CACHE_POSITIONS], previous_values)
    mixed = mixed + jnp.einsum('tbhgu,ubhd->tbhgd', weights[..., CACHE_POSITIONS:], new_values)
    decode_mix = mixed.astype(jnp.bfloat16).reshape(DECODE_STEPS, DECODE_SEQUENCES, HQ * HEAD_SIZE)
    live = finished * sequence_token_count
    live_rows = jnp.arange(POOLED_LENGTH, dtype=jnp.int32)[None, :] < live[:, None]
    masked = jnp.where(live_rows[:, :, None], pooled_layer_input, jnp.zeros((), jnp.bfloat16))
    seq_weight = finished.astype(jnp.float32) * advantages.astype(jnp.float32) / sequence_token_count.astype(jnp.float32)
    row_weight = jnp.where(live_rows, seq_weight[:, None], jnp.float32(0.0))
    scaled_rows = (row_weight[:, :, None] * pooled_value_gradient.astype(jnp.float32)).astype(jnp.bfloat16)
    replica = jnp.arange(POOLED_SEQUENCES, dtype=jnp.int32) // POOL
    offsets = (destinations - replica) % N_DP
    grid = offsets.reshape(N_DP, POOL)
    index = jnp.arange(POOL, dtype=jnp.int32)
    earlier = (grid[:, :, None] == grid[:, None, :]) & (index[None, None, :] < index[None, :, None])
    slot = lax.optimization_barrier(jnp.sum(earlier.astype(jnp.int32), axis=2)).reshape(POOLED_SEQUENCES)
    write_position = ((destinations * OFFS + offsets) * SLOTS + slot).astype(jnp.int32)
    input_rows = jnp.zeros((POOLED_SEQUENCES, POOLED_LENGTH, MODEL_WIDTH), jnp.bfloat16).at[write_position].set(masked).reshape(LEARNER_TOKENS, MODEL_WIDTH)
    gradient_rows = jnp.zeros((POOLED_SEQUENCES, POOLED_LENGTH, KEY_VALUE_HEADS * HEAD_SIZE), jnp.bfloat16).at[write_position].set(scaled_rows).reshape(LEARNER_TOKENS, KEY_VALUE_HEADS * HEAD_SIZE)
    latent_state = jnp.dot(input_rows, adapter_down_weight, preferred_element_type=jnp.float32).astype(jnp.bfloat16)
    trainer_value_rows = (jnp.dot(input_rows, frozen_value_weight, preferred_element_type=jnp.float32) + jnp.dot(latent_state, adapter_up_weight, preferred_element_type=jnp.float32)).astype(jnp.bfloat16)
    head_gradient = jnp.dot(gradient_rows, adapter_up_weight.T, preferred_element_type=jnp.float32).astype(jnp.bfloat16)
    grad_up = jnp.dot(latent_state.T, gradient_rows, preferred_element_type=jnp.float32)
    grad_down = jnp.dot(input_rows.T, head_gradient, preferred_element_type=jnp.float32).reshape(N_TP, MODEL_WIDTH // N_TP, ADAPTER_RANK)
    return (decode_mix, trainer_value_rows, grad_down, grad_up)
```

```python
import jax
import jax.numpy as jnp
from jax import lax
from jax.sharding import PartitionSpec as P

HEAD_SIZE = 128
OFFS = 4
SLOTS = 3
CACHE_POSITIONS = 256
POOLED_LENGTH = 16
QUERY_GROUP = 8
POOL = 12


def passed_along(array, axis, by):
    length = lax.axis_size(axis)
    return lax.ppermute(array, axis, [(i, (i + by) % length) for i in range(length)])


def stage_masks(n):
    bits = n.bit_length() - 1
    assert 1 << bits == n
    return [1 << k for k in range(bits)]


def bit_reversed(array, n):
    bits = n.bit_length() - 1
    rest = array.shape[1:]
    shaped = array.reshape((2,) * bits + rest)
    order = tuple(reversed(range(bits))) + tuple(range(bits, bits + len(rest)))
    return jnp.transpose(shaped, order).reshape((n,) + rest)


def butterfly_reduce_scatter(buf, axis, extra=None):
    n = lax.axis_size(axis)
    me = lax.axis_index(axis)
    for mask in stage_masks(n):
        half = buf.shape[0] // 2
        bit = (me // mask) % 2
        keep = lax.dynamic_slice_in_dim(buf, bit * half, half, axis=0)
        send = lax.dynamic_slice_in_dim(buf, (1 - bit) * half, half, axis=0)
        pairs = [(i, i ^ mask) for i in range(n)]
        if extra is None:
            buf = keep + lax.ppermute(send, axis, pairs)
        else:
            got, got_extra = lax.ppermute((send, extra), axis, pairs)
            buf = keep + got
            extra = extra + got_extra
    return buf[0], extra


def body(
    decode_step_input,
    query_key_value_weight,
    stored_keys,
    stored_values,
    stored_lengths,
    pooled_layer_input,
    pooled_value_gradient,
    finished,
    sequence_token_count,
    destinations,
    advantages,
    frozen_value_weight,
    adapter_down_weight,
    adapter_up_weight,
):
    n_dp = lax.axis_size("dp")
    n_tp = lax.axis_size("tp")
    step_count = decode_step_input.shape[0]
    width = decode_step_input.shape[2]
    rows_here = query_key_value_weight.shape[0]
    kv_local = stored_keys.shape[2] // HEAD_SIZE

    chunks = jnp.transpose(
        decode_step_input.reshape(step_count, n_dp, rows_here), (1, 0, 2)
    )
    spread = lax.all_to_all(chunks, "dp", 0, 0, tiled=True)
    spread = bit_reversed(spread, n_dp)
    partial = jnp.einsum(
        "bsr,rc->bsc", spread, query_key_value_weight, preferred_element_type=jnp.float32
    )
    projected, _ = butterfly_reduce_scatter(partial, "dp")
    projected_rows = projected.astype(jnp.bfloat16).reshape(
        1, step_count, kv_local, QUERY_GROUP + 2, HEAD_SIZE
    )
    local_seqs = 1
    queries = projected_rows[:, :, :, :QUERY_GROUP, :]
    fresh_keys = projected_rows[:, :, :, QUERY_GROUP, :]
    fresh_values = projected_rows[:, :, :, QUERY_GROUP + 1, :]
    previous_keys = stored_keys.reshape(local_seqs, CACHE_POSITIONS, kv_local, HEAD_SIZE)
    previous_values = stored_values.reshape(local_seqs, CACHE_POSITIONS, kv_local, HEAD_SIZE)
    scale = 1.0 / jnp.sqrt(jnp.float32(HEAD_SIZE))
    cached = (
        jnp.einsum("bthgd,bphd->bthgp", queries, previous_keys, preferred_element_type=jnp.float32)
        * scale
    )
    valid = jnp.arange(CACHE_POSITIONS, dtype=jnp.int32)[None, :] < stored_lengths[:, None]
    cached = jnp.where(valid[:, None, None, None, :], cached, jnp.float32(-1e30))
    recent = (
        jnp.einsum("bthgd,buhd->bthgu", queries, fresh_keys, preferred_element_type=jnp.float32)
        * scale
    )
    causal = (
        jnp.arange(step_count, dtype=jnp.int32)[None, :]
        <= jnp.arange(step_count, dtype=jnp.int32)[:, None]
    )
    recent = jnp.where(causal[None, :, None, None, :], recent, jnp.float32(-1e30))
    highest = jnp.maximum(jnp.max(cached, axis=-1), jnp.max(recent, axis=-1))[..., None]
    cached_exp = jnp.exp(cached - highest)
    recent_exp = jnp.exp(recent - highest)
    total = jnp.sum(cached_exp, axis=-1, keepdims=True) + jnp.sum(
        recent_exp, axis=-1, keepdims=True
    )
    cached_weights = (cached_exp / total).astype(jnp.bfloat16)
    recent_weights = (recent_exp / total).astype(jnp.bfloat16)
    mixed = jnp.einsum(
        "bthgp,bphd->bthgd", cached_weights, previous_values, preferred_element_type=jnp.float32
    )
    mixed = mixed + jnp.einsum(
        "bthgu,buhd->bthgd", recent_weights, fresh_values, preferred_element_type=jnp.float32
    )
    decode_mix = jnp.transpose(mixed.astype(jnp.bfloat16), (1, 0, 2, 3, 4)).reshape(
        step_count, local_seqs, kv_local * QUERY_GROUP * HEAD_SIZE
    )

    replica = lax.axis_index("dp")
    feature_slab = pooled_layer_input.shape[2]
    value_cols = pooled_value_gradient.shape[2]
    offsets = (destinations - replica) % n_dp
    write_position = jnp.arange(POOL, dtype=jnp.int32)
    earlier = (offsets[:, None] == offsets[None, :]) & (
        write_position[None, :] < write_position[:, None]
    )
    slot_index = jnp.sum(earlier.astype(jnp.int32), axis=1)
    packed_order = offsets * SLOTS + slot_index
    source_index = jnp.sum(
        jnp.where(packed_order[None, :] == write_position[:, None], write_position[None, :], 0),
        axis=1,
    )
    live_length = finished * sequence_token_count
    live_rows = jnp.arange(POOLED_LENGTH, dtype=jnp.int32)[None, :] < live_length[:, None]
    masked_hidden = jnp.where(
        live_rows[:, :, None], pooled_layer_input, jnp.zeros((), jnp.bfloat16)
    )
    seq_weight = (
        finished.astype(jnp.float32) * advantages / sequence_token_count.astype(jnp.float32)
    )
    row_weight = jnp.where(live_rows, seq_weight[:, None], jnp.float32(0.0))
    scaled_grad = (row_weight[:, :, None] * pooled_value_gradient.astype(jnp.float32)).astype(
        jnp.bfloat16
    )
    both = jnp.concatenate([masked_hidden, scaled_grad], axis=2)
    parcel = jnp.take(both, source_index, axis=0).reshape(
        OFFS, SLOTS, POOLED_LENGTH, feature_slab + value_cols
    )
    arrived = [parcel[0]]
    for offset in range(1, OFFS):
        arrived.append(passed_along(parcel[offset], "dp", offset))
    learner_rows = OFFS * SLOTS * POOLED_LENGTH
    local_rows = jnp.stack(arrived).reshape(learner_rows, feature_slab + value_cols)
    x_local = local_rows[:, :feature_slab]
    gradient_local = local_rows[:, feature_slab:]

    gathered = lax.all_gather(local_rows, "tp", axis=0, tiled=False)
    x_parts = gathered[:, :, :feature_slab]
    g_parts = gathered[:, :, feature_slab:]
    up_parts = lax.all_gather(adapter_up_weight, "tp", axis=0, tiled=False)
    value_rows = frozen_value_weight.shape[0]
    value_accumulator = jnp.einsum(
        "trf,tfc->rc",
        x_parts,
        frozen_value_weight.reshape(n_tp, value_rows // n_tp, -1),
        preferred_element_type=jnp.float32,
    )
    latent_state = jnp.einsum(
        "trf,tfk->rk",
        x_parts,
        adapter_down_weight.reshape(n_tp, value_rows // n_tp, -1),
        preferred_element_type=jnp.float32,
    ).astype(jnp.bfloat16)
    head_total = jnp.einsum(
        "trc,tkc->rk", g_parts, up_parts, preferred_element_type=jnp.float32
    ).astype(jnp.bfloat16)
    trainer_value_rows = (
        value_accumulator
        + jnp.dot(latent_state, adapter_up_weight, preferred_element_type=jnp.float32)
    ).astype(jnp.bfloat16)
    up_local = jnp.dot(latent_state.T, gradient_local, preferred_element_type=jnp.float32)
    down_local = lax.dot_general(
        x_local, head_total, (((0,), (0,)), ((), ())), preferred_element_type=jnp.float32
    )
    down_blocks = bit_reversed(down_local.reshape(n_dp, feature_slab // n_dp, -1), n_dp)
    grad_down, grad_up = butterfly_reduce_scatter(down_blocks, "dp", extra=up_local)
    return (decode_mix, trainer_value_rows, grad_down[None], grad_up)


def solution(mesh):
    in_specs = (
        P(None, "dp", None),
        P("dp", "tp"),
        P("dp", None, "tp"),
        P("dp", None, "tp"),
        P("dp"),
        P("dp", None, "tp"),
        P("dp", None, "tp"),
        P("dp"),
        P("dp"),
        P("dp"),
        P("dp"),
        P(None, "tp"),
        P(),
        P(None, "tp"),
    )
    out_specs = (P(None, "dp", "tp"), P("dp", "tp"), P("tp", "dp", None), P(None, "tp"))
    return jax.shard_map(body, mesh=mesh, in_specs=in_specs, out_specs=out_specs, check_vma=False)
```

```python
import jax
import jax.numpy as jnp
from jax import lax
from jax.sharding import PartitionSpec as P

HEAD_SIZE = 128
OFFS = 4
SLOTS = 3
CACHE_POSITIONS = 256
POOLED_LENGTH = 16
QUERY_GROUP = 8
POOL = 12


def passed_along(array, axis, by):
    length = lax.axis_size(axis)
    return lax.ppermute(array, axis, [(i, (i + by) % length) for i in range(length)])


def stage_masks(n):
    bits = n.bit_length() - 1
    assert 1 << bits == n
    return [1 << k for k in range(bits)]


def bit_reversed(array, n):
    bits = n.bit_length() - 1
    rest = array.shape[1:]
    shaped = array.reshape((2,) * bits + rest)
    order = tuple(reversed(range(bits))) + tuple(range(bits, bits + len(rest)))
    return jnp.transpose(shaped, order).reshape((n,) + rest)


def butterfly_reduce_scatter(buf, axis, extra=None):
    n = lax.axis_size(axis)
    me = lax.axis_index(axis)
    for mask in stage_masks(n):
        half = buf.shape[0] // 2
        bit = (me // mask) % 2
        keep = lax.dynamic_slice_in_dim(buf, bit * half, half, axis=0)
        send = lax.dynamic_slice_in_dim(buf, (1 - bit) * half, half, axis=0)
        pairs = [(i, i ^ mask) for i in range(n)]
        if extra is None:
            buf = keep + lax.ppermute(send, axis, pairs)
        else:
            lanes = extra.shape[-1]
            message = jnp.concatenate([send.reshape(-1, lanes), extra], axis=0)
            got = lax.ppermute(message, axis, pairs)
            split = send.size // lanes
            buf = keep + got[:split].reshape(send.shape)
            extra = extra + got[split:]
    return buf[0], extra


def butterfly_all_reduce(value, axis):
    n = lax.axis_size(axis)
    for mask in stage_masks(n):
        value = value + lax.ppermute(value, axis, [(i, i ^ mask) for i in range(n)])
    return value


def body(
    decode_step_input,
    query_key_value_weight,
    stored_keys,
    stored_values,
    stored_lengths,
    pooled_layer_input,
    pooled_value_gradient,
    finished,
    sequence_token_count,
    destinations,
    advantages,
    frozen_value_weight,
    adapter_down_weight,
    adapter_up_weight,
):
    n_dp = lax.axis_size("dp")
    n_tp = lax.axis_size("tp")
    step_count = decode_step_input.shape[0]
    rows_here = query_key_value_weight.shape[0]
    kv_local = stored_keys.shape[2] // HEAD_SIZE

    chunks = jnp.transpose(
        decode_step_input.reshape(step_count, n_dp, rows_here), (1, 0, 2)
    )
    spread = lax.all_to_all(chunks, "dp", 0, 0, tiled=True)
    spread = bit_reversed(spread, n_dp)
    partial = jnp.einsum(
        "bsr,rc->bsc", spread, query_key_value_weight, preferred_element_type=jnp.float32
    )
    partial_blocks = partial.reshape(n_dp, -1)

    replica = lax.axis_index("dp")
    feature_slab = pooled_layer_input.shape[2]
    value_cols = pooled_value_gradient.shape[2]
    offsets = (destinations - replica) % n_dp
    write_position = jnp.arange(POOL, dtype=jnp.int32)
    earlier = (offsets[:, None] == offsets[None, :]) & (
        write_position[None, :] < write_position[:, None]
    )
    slot_index = jnp.sum(earlier.astype(jnp.int32), axis=1)
    packed_order = offsets * SLOTS + slot_index
    source_index = jnp.sum(
        jnp.where(packed_order[None, :] == write_position[:, None], write_position[None, :], 0),
        axis=1,
    )
    live_length = finished * sequence_token_count
    live_rows = jnp.arange(POOLED_LENGTH, dtype=jnp.int32)[None, :] < live_length[:, None]
    masked_hidden = jnp.where(
        live_rows[:, :, None], pooled_layer_input, jnp.zeros((), jnp.bfloat16)
    )
    seq_weight = (
        finished.astype(jnp.float32) * advantages / sequence_token_count.astype(jnp.float32)
    )
    row_weight = jnp.where(live_rows, seq_weight[:, None], jnp.float32(0.0))
    scaled_grad = (row_weight[:, :, None] * pooled_value_gradient.astype(jnp.float32)).astype(
        jnp.bfloat16
    )
    both = jnp.concatenate([masked_hidden, scaled_grad], axis=2)
    parcel = jnp.take(both, source_index, axis=0).reshape(
        OFFS, SLOTS, POOLED_LENGTH, feature_slab + value_cols
    )
    arrived = [parcel[0]]
    for offset in range(1, OFFS):
        arrived.append(passed_along(parcel[offset], "dp", offset))
    learner_rows = OFFS * SLOTS * POOLED_LENGTH
    local_rows = jnp.stack(arrived).reshape(learner_rows, feature_slab + value_cols)
    x_local = local_rows[:, :feature_slab]
    gradient_local = local_rows[:, feature_slab:]

    head_index = lax.axis_index("tp")
    down_slab = lax.dynamic_slice_in_dim(
        adapter_down_weight, head_index * feature_slab, feature_slab, axis=0
    )
    latent_part = jnp.dot(x_local, down_slab, preferred_element_type=jnp.float32)
    head_part = jnp.dot(gradient_local, adapter_up_weight.T, preferred_element_type=jnp.float32)
    summed = butterfly_all_reduce(jnp.concatenate([latent_part, head_part], axis=1), "tp")
    rank = latent_part.shape[1]
    latent_state = summed[:, :rank].astype(jnp.bfloat16)
    head_total = summed[:, rank:].astype(jnp.bfloat16)

    up_local = jnp.dot(latent_state.T, gradient_local, preferred_element_type=jnp.float32)
    down_local = lax.dot_general(
        x_local, head_total, (((0,), (0,)), ((), ())), preferred_element_type=jnp.float32
    )
    down_blocks = bit_reversed(down_local.reshape(n_dp, -1), n_dp)
    reduced, grad_up = butterfly_reduce_scatter(
        jnp.concatenate([partial_blocks, down_blocks], axis=1), "dp", extra=up_local
    )
    projected = reduced[: partial_blocks.shape[1]].reshape(step_count, -1)
    grad_down = reduced[partial_blocks.shape[1] :].reshape(feature_slab // n_dp, rank)

    gathered = lax.all_gather(x_local, "tp", axis=0, tiled=False)
    value_rows = frozen_value_weight.shape[0]
    value_accumulator = jnp.einsum(
        "trf,tfc->rc",
        gathered,
        frozen_value_weight.reshape(n_tp, value_rows // n_tp, -1),
        preferred_element_type=jnp.float32,
    )
    trainer_value_rows = (
        value_accumulator
        + jnp.dot(latent_state, adapter_up_weight, preferred_element_type=jnp.float32)
    ).astype(jnp.bfloat16)

    projected_rows = projected.astype(jnp.bfloat16).reshape(
        1, step_count, kv_local, QUERY_GROUP + 2, HEAD_SIZE
    )
    local_seqs = 1
    queries = projected_rows[:, :, :, :QUERY_GROUP, :]
    fresh_keys = projected_rows[:, :, :, QUERY_GROUP, :]
    fresh_values = projected_rows[:, :, :, QUERY_GROUP + 1, :]
    previous_keys = stored_keys.reshape(local_seqs, CACHE_POSITIONS, kv_local, HEAD_SIZE)
    previous_values = stored_values.reshape(local_seqs, CACHE_POSITIONS, kv_local, HEAD_SIZE)
    scale = 1.0 / jnp.sqrt(jnp.float32(HEAD_SIZE))
    cached = (
        jnp.einsum("bthgd,bphd->bthgp", queries, previous_keys, preferred_element_type=jnp.float32)
        * scale
    )
    valid = jnp.arange(CACHE_POSITIONS, dtype=jnp.int32)[None, :] < stored_lengths[:, None]
    cached = jnp.where(valid[:, None, None, None, :], cached, jnp.float32(-1e30))
    recent = (
        jnp.einsum("bthgd,buhd->bthgu", queries, fresh_keys, preferred_element_type=jnp.float32)
        * scale
    )
    causal = (
        jnp.arange(step_count, dtype=jnp.int32)[None, :]
        <= jnp.arange(step_count, dtype=jnp.int32)[:, None]
    )
    recent = jnp.where(causal[None, :, None, None, :], recent, jnp.float32(-1e30))
    highest = jnp.maximum(jnp.max(cached, axis=-1), jnp.max(recent, axis=-1))[..., None]
    cached_exp = jnp.exp(cached - highest)
    recent_exp = jnp.exp(recent - highest)
    total = jnp.sum(cached_exp, axis=-1, keepdims=True) + jnp.sum(
        recent_exp, axis=-1, keepdims=True
    )
    cached_weights = (cached_exp / total).astype(jnp.bfloat16)
    recent_weights = (recent_exp / total).astype(jnp.bfloat16)
    mixed = jnp.einsum(
        "bthgp,bphd->bthgd", cached_weights, previous_values, preferred_element_type=jnp.float32
    )
    mixed = mixed + jnp.einsum(
        "bthgu,buhd->bthgd", recent_weights, fresh_values, preferred_element_type=jnp.float32
    )
    decode_mix = jnp.transpose(mixed.astype(jnp.bfloat16), (1, 0, 2, 3, 4)).reshape(
        step_count, local_seqs, kv_local * QUERY_GROUP * HEAD_SIZE
    )

    return (decode_mix, trainer_value_rows, grad_down[None], grad_up)


def solution(mesh):
    in_specs = (
        P(None, "dp", None),
        P("dp", "tp"),
        P("dp", None, "tp"),
        P("dp", None, "tp"),
        P("dp"),
        P("dp", None, "tp"),
        P("dp", None, "tp"),
        P("dp"),
        P("dp"),
        P("dp"),
        P("dp"),
        P(None, "tp"),
        P(),
        P(None, "tp"),
    )
    out_specs = (P(None, "dp", "tp"), P("dp", "tp"), P("tp", "dp", None), P(None, "tp"))
    return jax.shard_map(body, mesh=mesh, in_specs=in_specs, out_specs=out_specs, check_vma=False)
```

```python
import jax
import jax.numpy as jnp
from jax import lax
from jax.sharding import PartitionSpec as P

HEAD_SIZE = 128
OFFS = 4
SLOTS = 3
CACHE_POSITIONS = 256
POOLED_LENGTH = 16
QUERY_GROUP = 8
POOL = 12


def passed_along(array, axis, by):
    length = lax.axis_size(axis)
    return lax.ppermute(array, axis, [(i, (i + by) % length) for i in range(length)])


def stage_masks(n):
    bits = n.bit_length() - 1
    assert 1 << bits == n
    return [1 << k for k in range(bits)]


def bit_reversed(array, n):
    bits = n.bit_length() - 1
    rest = array.shape[1:]
    shaped = array.reshape((2,) * bits + rest)
    order = tuple(reversed(range(bits))) + tuple(range(bits, bits + len(rest)))
    return jnp.transpose(shaped, order).reshape((n,) + rest)


def butterfly_reduce_scatter(buf, axis, extra=None):
    n = lax.axis_size(axis)
    me = lax.axis_index(axis)
    for mask in stage_masks(n):
        half = buf.shape[0] // 2
        bit = (me // mask) % 2
        keep = lax.dynamic_slice_in_dim(buf, bit * half, half, axis=0)
        send = lax.dynamic_slice_in_dim(buf, (1 - bit) * half, half, axis=0)
        pairs = [(i, i ^ mask) for i in range(n)]
        if extra is None:
            buf = keep + lax.ppermute(send, axis, pairs)
        else:
            lanes = extra.shape[-1]
            message = jnp.concatenate([send.reshape(-1, lanes), extra], axis=0)
            got = lax.ppermute(message, axis, pairs)
            split = send.size // lanes
            buf = keep + got[:split].reshape(send.shape)
            extra = extra + got[split:]
    return buf[0], extra


def butterfly_all_reduce(value, axis):
    n = lax.axis_size(axis)
    for mask in stage_masks(n):
        value = value + lax.ppermute(value, axis, [(i, i ^ mask) for i in range(n)])
    return value


def body(
    decode_step_input,
    query_key_value_weight,
    stored_keys,
    stored_values,
    stored_lengths,
    pooled_layer_input,
    pooled_value_gradient,
    finished,
    sequence_token_count,
    destinations,
    advantages,
    frozen_value_weight,
    adapter_down_weight,
    adapter_up_weight,
):
    n_dp = lax.axis_size("dp")
    n_tp = lax.axis_size("tp")
    step_count = decode_step_input.shape[0]
    rows_here = query_key_value_weight.shape[0]
    kv_local = stored_keys.shape[2] // HEAD_SIZE

    chunks = jnp.transpose(
        decode_step_input.reshape(step_count, n_dp, rows_here), (1, 0, 2)
    )
    spread = lax.all_to_all(chunks, "dp", 0, 0, tiled=True)
    spread = bit_reversed(spread, n_dp)
    partial = jnp.einsum(
        "bsr,rc->bsc", spread, query_key_value_weight, preferred_element_type=jnp.float32
    )
    partial_blocks = partial.reshape(n_dp, -1, HEAD_SIZE)

    replica = lax.axis_index("dp")
    feature_slab = pooled_layer_input.shape[2]
    value_cols = pooled_value_gradient.shape[2]
    offsets = (destinations - replica) % n_dp
    write_position = jnp.arange(POOL, dtype=jnp.int32)
    earlier = (offsets[:, None] == offsets[None, :]) & (
        write_position[None, :] < write_position[:, None]
    )
    slot_index = jnp.sum(earlier.astype(jnp.int32), axis=1)
    packed_order = offsets * SLOTS + slot_index
    source_index = jnp.sum(
        jnp.where(packed_order[None, :] == write_position[:, None], write_position[None, :], 0),
        axis=1,
    )
    live_length = finished * sequence_token_count
    live_rows = jnp.arange(POOLED_LENGTH, dtype=jnp.int32)[None, :] < live_length[:, None]
    masked_hidden = jnp.where(
        live_rows[:, :, None], pooled_layer_input, jnp.zeros((), jnp.bfloat16)
    )
    seq_weight = (
        finished.astype(jnp.float32) * advantages / sequence_token_count.astype(jnp.float32)
    )
    row_weight = jnp.where(live_rows, seq_weight[:, None], jnp.float32(0.0))
    scaled_grad = (row_weight[:, :, None] * pooled_value_gradient.astype(jnp.float32)).astype(
        jnp.bfloat16
    )
    both = jnp.concatenate([masked_hidden, scaled_grad], axis=2)
    parcel = jnp.take(both, source_index, axis=0).reshape(
        OFFS, SLOTS, POOLED_LENGTH, feature_slab + value_cols
    )
    arrived = [parcel[0]]
    for offset in range(1, OFFS):
        arrived.append(passed_along(parcel[offset], "dp", offset))
    learner_rows = OFFS * SLOTS * POOLED_LENGTH
    local_rows = jnp.stack(arrived).reshape(learner_rows, feature_slab + value_cols)
    x_local = local_rows[:, :feature_slab]
    gradient_local = local_rows[:, feature_slab:]

    head_index = lax.axis_index("tp")
    down_slab = lax.dynamic_slice_in_dim(
        adapter_down_weight, head_index * feature_slab, feature_slab, axis=0
    )
    latent_part = jnp.dot(x_local, down_slab, preferred_element_type=jnp.float32)
    head_part = jnp.dot(gradient_local, adapter_up_weight.T, preferred_element_type=jnp.float32)
    summed = butterfly_all_reduce(jnp.concatenate([latent_part, head_part], axis=1), "tp")
    rank = latent_part.shape[1]
    latent_state = summed[:, :rank].astype(jnp.bfloat16)
    head_total = summed[:, rank:].astype(jnp.bfloat16)

    up_local = jnp.dot(latent_state.T, gradient_local, preferred_element_type=jnp.float32)
    down_local = lax.dot_general(
        x_local, head_total, (((0,), (0,)), ((), ())), preferred_element_type=jnp.float32
    )
    lanes = up_local.shape[1]
    down_blocks = bit_reversed(
        down_local.reshape(n_dp, feature_slab // n_dp, rank), n_dp
    ).reshape(n_dp, -1, lanes)
    used_rows = partial_blocks.shape[1] + down_blocks.shape[1]
    pad_rows = -used_rows % 8
    blocks = jnp.concatenate(
        [partial_blocks, down_blocks, jnp.zeros((n_dp, pad_rows, lanes), jnp.float32)], axis=1
    )
    reduced, grad_up = butterfly_reduce_scatter(blocks, "dp", extra=up_local)
    projected = reduced[: partial_blocks.shape[1]].reshape(step_count, -1)
    grad_down = reduced[partial_blocks.shape[1] : used_rows].reshape(feature_slab // n_dp, rank)

    gathered = lax.all_gather(x_local, "tp", axis=0, tiled=False)
    value_rows = frozen_value_weight.shape[0]
    value_accumulator = jnp.einsum(
        "trf,tfc->rc",
        gathered,
        frozen_value_weight.reshape(n_tp, value_rows // n_tp, -1),
        preferred_element_type=jnp.float32,
    )
    trainer_value_rows = (
        value_accumulator
        + jnp.dot(latent_state, adapter_up_weight, preferred_element_type=jnp.float32)
    ).astype(jnp.bfloat16)

    projected_rows = projected.astype(jnp.bfloat16).reshape(
        1, step_count, kv_local, QUERY_GROUP + 2, HEAD_SIZE
    )
    local_seqs = 1
    queries = projected_rows[:, :, :, :QUERY_GROUP, :]
    fresh_keys = projected_rows[:, :, :, QUERY_GROUP, :]
    fresh_values = projected_rows[:, :, :, QUERY_GROUP + 1, :]
    previous_keys = stored_keys.reshape(local_seqs, CACHE_POSITIONS, kv_local, HEAD_SIZE)
    previous_values = stored_values.reshape(local_seqs, CACHE_POSITIONS, kv_local, HEAD_SIZE)
    scale = 1.0 / jnp.sqrt(jnp.float32(HEAD_SIZE))
    cached = (
        jnp.einsum("bthgd,bphd->bthgp", queries, previous_keys, preferred_element_type=jnp.float32)
        * scale
    )
    valid = jnp.arange(CACHE_POSITIONS, dtype=jnp.int32)[None, :] < stored_lengths[:, None]
    cached = jnp.where(valid[:, None, None, None, :], cached, jnp.float32(-1e30))
    recent = (
        jnp.einsum("bthgd,buhd->bthgu", queries, fresh_keys, preferred_element_type=jnp.float32)
        * scale
    )
    causal = (
        jnp.arange(step_count, dtype=jnp.int32)[None, :]
        <= jnp.arange(step_count, dtype=jnp.int32)[:, None]
    )
    recent = jnp.where(causal[None, :, None, None, :], recent, jnp.float32(-1e30))
    highest = jnp.maximum(jnp.max(cached, axis=-1), jnp.max(recent, axis=-1))[..., None]
    cached_exp = jnp.exp(cached - highest)
    recent_exp = jnp.exp(recent - highest)
    total = jnp.sum(cached_exp, axis=-1, keepdims=True) + jnp.sum(
        recent_exp, axis=-1, keepdims=True
    )
    cached_weights = (cached_exp / total).astype(jnp.bfloat16)
    recent_weights = (recent_exp / total).astype(jnp.bfloat16)
    mixed = jnp.einsum(
        "bthgp,bphd->bthgd", cached_weights, previous_values, preferred_element_type=jnp.float32
    )
    mixed = mixed + jnp.einsum(
        "bthgu,buhd->bthgd", recent_weights, fresh_values, preferred_element_type=jnp.float32
    )
    decode_mix = jnp.transpose(mixed.astype(jnp.bfloat16), (1, 0, 2, 3, 4)).reshape(
        step_count, local_seqs, kv_local * QUERY_GROUP * HEAD_SIZE
    )

    return (decode_mix, trainer_value_rows, grad_down[None], grad_up)


def solution(mesh):
    in_specs = (
        P(None, "dp", None),
        P("dp", "tp"),
        P("dp", None, "tp"),
        P("dp", None, "tp"),
        P("dp"),
        P("dp", None, "tp"),
        P("dp", None, "tp"),
        P("dp"),
        P("dp"),
        P("dp"),
        P("dp"),
        P(None, "tp"),
        P(),
        P(None, "tp"),
    )
    out_specs = (P(None, "dp", "tp"), P("dp", "tp"), P("tp", "dp", None), P(None, "tp"))
    return jax.shard_map(body, mesh=mesh, in_specs=in_specs, out_specs=out_specs, check_vma=False)
```
